1024 devices in a mesh: row: 16 (over x, core), col: 64 (over z, y).
Axes of the slice: x: 8, y: 8, z: 8, core: 2. Of those that a mesh axis runs over, the one named last changes fastest.
Arguments:
- states: bfloat16 [131072, 384], P(('row', 'col')), may hold values from -6 to 6
- mix_weight: bfloat16 [384, 384], replicated, may hold values from -0.3125 to 0.3125
- coherence: bfloat16 [16, 64, 32, 128, 128], P('row', 'col'), may hold values from -0.125 to 0.125
- block_row: int32 [16, 64, 32], P('row', 'col'), may hold values from 0 to 15, as said below
- block_col: int32 [16, 64, 32], P('row', 'col'), may hold values from 0 to 15
- block_count: int32 [16, 64], P('row', 'col'), may hold values from 8 to 32, as said below
- gain: float32 [384], replicated, may hold values from 0.5 to 1.5
- bias: float32 [384], replicated, may hold values from -3 to 3
Outputs:
- linked: bfloat16 [131072, 384], P(('row', 'col'))
The draws below stay inside these ranges and needn't reach their ends.
Inputs may be any that keep to these rules, and one draw needn't show every extreme that they name: `block_count`: no device has more than 32 live slots, and some device has exactly 32. `block_row`: at most 2 of one device's slots name any one block row; in each column group some block row is named by 2 live slots of every device.
All inputs are finite; a program needn't handle non-finite values.
Results may differ from the reference program's by a relative error of at most 0.014.
Values may be sent and summed in bfloat16 or wider, within the bound.
No kernel may reach another device: no remote copies, remote signals or barrier semaphores. Data moves between devices by JAX's collectives and lax.ppermute only.
A program may use at most 32 MiB of HBM per device.

```python
import jax
import jax.numpy as jnp
from jax import lax

H = 384
BLK = 128
MAXB = 32
ITERS = 2
CAP = 2
NC = 131072
N_ROW = 16
N_COL = 64


def draw_block_row(key, part):
    first_key, second_key, third_key = jax.random.split(jax.random.fold_in(key, 17), 3)
    chosen = jax.random.randint(first_key, (N_COL,), 0, N_ROW)
    row_iota = jnp.arange(N_ROW, dtype=jnp.int32)
    row_scores = jax.random.randint(second_key, (N_ROW, N_COL, N_ROW), 0, 1048576) * N_ROW + row_iota
    row_scores = jnp.where(row_iota[None, None, :] == chosen[None, :, None], -1, row_scores)
    row_order = jnp.argsort(row_scores, axis=-1, stable=True).astype(jnp.int32)
    seat_group = jnp.arange(MAXB, dtype=jnp.int32) // CAP
    seat_rows = jnp.take_along_axis(row_order, jnp.broadcast_to(seat_group, (N_ROW, N_COL, MAXB)), axis=-1)
    slot_iota = jnp.arange(MAXB, dtype=jnp.int32)
    slot_scores = jax.random.randint(third_key, (N_ROW, N_COL, MAXB), 0, 1048576) * MAXB + slot_iota
    slot_scores = jnp.where(slot_iota[None, None, :] < CAP, -1 - (CAP - slot_iota[None, None, :]), slot_scores)
    slot_order = jnp.argsort(slot_scores, axis=-1, stable=True).astype(jnp.int32)
    return jnp.take_along_axis(seat_rows, slot_order, axis=-1).astype(jnp.int32)


def draw_block_count(key, part):
    first_key, second_key, third_key = jax.random.split(key, 3)
    divisor = jax.random.randint(first_key, (N_ROW, N_COL), 1, 5)
    counts = jnp.maximum(MAXB // divisor, CAP).astype(jnp.int32)
    row_pick = jax.random.randint(second_key, (), 0, N_ROW)
    col_pick = jax.random.randint(third_key, (), 0, N_COL)
    return counts.at[row_pick, col_pick].set(MAXB).astype(jnp.int32)


def touch_ends(array, rng, least, high):
    dims = array.shape
    place = [jax.random.randint(jax.random.fold_in(rng, axis), (), 0, dims[axis]) for axis in range(len(dims))]
    array = array.at[tuple(place)].set(least)
    longest = dims.index(max(dims))
    place[longest] = (place[longest] + 1) % dims[longest]
    return array.at[tuple(place)].set(high)


def steps_of(key, extent, cuts, least, high):
    def one(dim, parts):
        steps = jax.random.uniform(jax.random.fold_in(jax.random.fold_in(key, 6), dim), (parts,), jnp.float32, least / len(cuts), high / len(cuts))
        return jnp.repeat(jnp.exp(steps), extent[dim] // parts).reshape((-1,) + (1,) * (len(extent) - dim - 1))

    factor_of = one(*cuts[0])
    for cut in cuts[1:]:
        factor_of = factor_of * one(*cut)
    return factor_of


def normal_values(stream_key, shape, width, most, cuts=(), kind=jnp.bfloat16):
    entries = jax.random.normal(stream_key, shape, jnp.float32) * width
    if len(cuts) > 0:
        entries = steps_of(stream_key, shape, cuts, -0.22, 0.18) * entries
    return jnp.clip(entries, min=-most, max=most).astype(kind)


def setup_inputs(seed: int = 0) -> dict:
    seeds = jax.random.split(jax.random.key(seed), 9)
    return {
        "states": normal_values(seeds[0], (NC, H), 1.0, 6.0, ((0, 1024),)),
        "mix_weight": normal_values(seeds[1], (H, H), H ** -0.5, 0.3125),
        "coherence": normal_values(seeds[2], (N_ROW, N_COL, MAXB, BLK, BLK), (MAXB * BLK // 2) ** -0.5, 0.125, ((0, 16), (1, 64))),
        "block_row": draw_block_row(jax.random.fold_in(seeds[8], 71), 0),
        "block_col": touch_ends(jax.random.randint(seeds[4], (N_ROW, N_COL, MAXB), 0, N_ROW), jax.random.fold_in(seeds[4], 1), 0, N_ROW - 1).astype(jnp.int32),
        "block_count": draw_block_count(jax.random.fold_in(seeds[8], 71), 0),
        "gain": jnp.clip(1.0 + 0.1 * jax.random.normal(seeds[6], (H,), jnp.float32), 0.5, 1.5),
        "bias": normal_values(seeds[7], (H,), 0.5, 3.0, (), jnp.float32),
    }


def normalize(hidden, coupled, gain, bias):
    summed_in = hidden.astype(jnp.float32) + coupled
    mean_value = lax.optimization_barrier(jnp.mean(summed_in, axis=-1, keepdims=True))
    centered = summed_in - mean_value
    variance = lax.optimization_barrier(jnp.mean(centered * centered, axis=-1, keepdims=True))
    return (centered * lax.rsqrt(variance + 1e-05) * gain + bias).astype(jnp.bfloat16)

def reference(states, mix_weight, coherence, block_row, block_col, block_count, gain, bias):
    slice_rows = BLK // N_COL
    grid_states = states.reshape(N_ROW, N_COL, N_COL, slice_rows, H)
    grid_states = jnp.transpose(grid_states, (2, 0, 1, 3, 4)).reshape(N_COL, N_ROW, BLK, H)
    slot_ids = jnp.arange(MAXB, dtype=jnp.int32)
    targets = jnp.arange(N_ROW, dtype=jnp.int32)
    blocks_t = jnp.transpose(coherence, (1, 0, 2, 3, 4))
    rows_t = jnp.transpose(block_row, (1, 0, 2))
    cols_t = jnp.transpose(block_col, (1, 0, 2))
    counts_t = jnp.transpose(block_count, (1, 0))

    def couple_group(group_args):
        mixed, blocks, row_ids, col_ids, counts = group_args
        pieces = mixed[col_ids].astype(jnp.float32)
        products_f = jnp.einsum('rkab,rkbh->rkah', blocks.astype(jnp.float32), pieces, precision=lax.Precision.HIGHEST)
        live_mask = slot_ids[None, :] < counts[:, None]
        onehot = ((row_ids[:, None, :] == targets[None, :, None]) & live_mask[:, None, :]).astype(jnp.float32)
        terms = jnp.einsum('rik,rkah->riah', onehot, products_f, precision=lax.Precision.HIGHEST).astype(jnp.bfloat16)
        return lax.optimization_barrier(jnp.sum(terms.astype(jnp.float32), axis=0))
    hidden = grid_states
    for iteration in range(ITERS):
        mixed = jnp.dot(hidden.reshape(-1, H), mix_weight, preferred_element_type=jnp.float32)
        mixed = mixed.astype(jnp.bfloat16).reshape(N_COL, N_ROW, BLK, H)
        coupled = lax.map(couple_group, (mixed, blocks_t, rows_t, cols_t, counts_t))
        hidden = normalize(hidden, coupled, gain, bias)
    restored = hidden.reshape(N_COL, N_ROW, N_COL, slice_rows, H)
    restored = jnp.transpose(restored, (1, 2, 0, 3, 4)).reshape(-1, H)
    return restored
```

```python
import jax
import jax.numpy as jnp
from jax import lax
from jax.sharding import PartitionSpec as P

ITERS = 2


def normalize(hidden, coupled, gain, bias):
    summed_in = hidden.astype(jnp.float32) + coupled
    mean_value = jnp.mean(summed_in, axis=-1, keepdims=True)
    centered = summed_in - mean_value
    variance = jnp.mean(centered * centered, axis=-1, keepdims=True)
    return (centered * lax.rsqrt(variance + 1e-05) * gain + bias).astype(jnp.bfloat16)


def to_grid(values):
    return lax.all_to_all(values, "col", split_axis=0, concat_axis=0, tiled=True)


def seat_layout(blocks, row_ids, col_ids, live_count, row_groups, seats_per_row):
    slot_total = row_ids.shape[0]
    block_len = blocks.shape[1]
    slot_ids = jnp.arange(slot_total, dtype=jnp.int32)
    live_mask = slot_ids < live_count
    earlier = (
        (row_ids[:, None] == row_ids[None, :])
        & (slot_ids[None, :] < slot_ids[:, None])
        & live_mask[None, :]
    )
    rank_in_row = jnp.sum(earlier.astype(jnp.int32), axis=1)
    seat_total = row_groups * seats_per_row
    seat_index = jnp.where(live_mask, row_ids * seats_per_row + rank_in_row, seat_total)
    seat_blocks = (
        jnp.zeros((seat_total, block_len, block_len), blocks.dtype)
        .at[seat_index]
        .set(blocks, mode="drop")
    )
    seat_cols = jnp.zeros((seat_total,), jnp.int32).at[seat_index].set(col_ids, mode="drop")
    return (
        seat_blocks.reshape(row_groups, seats_per_row, block_len, block_len),
        seat_cols.reshape(row_groups, seats_per_row),
    )


def couple(grid_mixed, owned_blocks, owned_cols):
    pieces_all = lax.all_gather(grid_mixed, "row", axis=0, tiled=False)
    pieces = pieces_all[owned_cols]
    per_source = jnp.einsum(
        "rsab,rsbh->rah", owned_blocks, pieces, preferred_element_type=jnp.float32
    )
    return jnp.sum(per_source.astype(jnp.bfloat16).astype(jnp.float32), axis=0)


def body(states, mix_weight, coherence, block_row, block_col, block_count, gain, bias):
    blocks = coherence[0, 0]
    row_ids = block_row[0, 0]
    col_ids = block_col[0, 0]
    live_count = block_count[0, 0]
    row_groups = lax.axis_size("row")
    slot_total = row_ids.shape[0]
    seats_per_row = max(2, (slot_total + row_groups - 1) // row_groups)
    seat_blocks, seat_cols = seat_layout(
        blocks, row_ids, col_ids, live_count, row_groups, seats_per_row
    )
    owned_blocks = lax.all_to_all(seat_blocks, "row", split_axis=0, concat_axis=0, tiled=True)
    owned_cols = lax.all_to_all(seat_cols, "row", split_axis=0, concat_axis=0, tiled=True)
    hidden = to_grid(states)
    for iteration in range(ITERS):
        mixed = jnp.dot(hidden, mix_weight, preferred_element_type=jnp.float32).astype(jnp.bfloat16)
        coupled = couple(mixed, owned_blocks, owned_cols)
        hidden = normalize(hidden, coupled, gain, bias)
    return to_grid(hidden)


def solution(mesh):
    placed = (
        P(("row", "col"), None),
        P(),
        P("row", "col", None, None, None),
        P("row", "col", None),
        P("row", "col", None),
        P("row", "col"),
        P(),
        P(),
    )
    return jax.shard_map(
        body, mesh=mesh, in_specs=placed, out_specs=P(("row", "col"), None), check_vma=False
    )
```

```python
import jax
import jax.numpy as jnp
from jax import lax
from jax.sharding import PartitionSpec as P

ITERS = 2


def normalize(hidden, coupled, gain, bias):
    summed_in = hidden.astype(jnp.float32) + coupled
    mean_value = jnp.mean(summed_in, axis=-1, keepdims=True)
    centered = summed_in - mean_value
    variance = jnp.mean(centered * centered, axis=-1, keepdims=True)
    return (centered * lax.rsqrt(variance + 1e-05) * gain + bias).astype(jnp.bfloat16)


def to_grid(values):
    col_hi = lax.axis_size("cz")
    col_lo = lax.axis_size("cy")
    rows = values.shape[0] // (col_hi * col_lo)
    parts = values.reshape(col_hi, col_lo, rows, values.shape[1])
    parts = lax.all_to_all(parts, "cy", split_axis=1, concat_axis=1, tiled=True)
    parts = lax.all_to_all(parts, "cz", split_axis=0, concat_axis=0, tiled=True)
    return parts.reshape(values.shape)


def seat_layout(blocks, row_ids, col_ids, live_count, row_groups, seats_per_row):
    slot_total = row_ids.shape[0]
    block_len = blocks.shape[1]
    slot_ids = jnp.arange(slot_total, dtype=jnp.int32)
    live_mask = slot_ids < live_count
    earlier = (
        (row_ids[:, None] == row_ids[None, :])
        & (slot_ids[None, :] < slot_ids[:, None])
        & live_mask[None, :]
    )
    rank_in_row = jnp.sum(earlier.astype(jnp.int32), axis=1)
    seat_total = row_groups * seats_per_row
    seat_index = jnp.where(live_mask, row_ids * seats_per_row + rank_in_row, seat_total)
    seat_blocks = (
        jnp.zeros((seat_total, block_len, block_len), blocks.dtype)
        .at[seat_index]
        .set(blocks, mode="drop")
    )
    seat_cols = jnp.zeros((seat_total,), jnp.int32).at[seat_index].set(col_ids, mode="drop")
    return (
        seat_blocks.reshape(row_groups, seats_per_row, block_len, block_len),
        seat_cols.reshape(row_groups, seats_per_row),
    )


def couple(grid_mixed, owned_blocks, owned_cols):
    pieces_all = lax.all_gather(grid_mixed, "rx", axis=0, tiled=False)
    pieces_all = lax.all_gather(pieces_all, "rc", axis=0, tiled=False)
    cores = lax.axis_size("rc")
    chips = lax.axis_size("rx")
    pieces_all = pieces_all.reshape((cores * chips,) + grid_mixed.shape)
    pieces = pieces_all[(owned_cols % cores) * chips + owned_cols // cores]
    per_source = jnp.einsum(
        "rsab,rsbh->rah", owned_blocks, pieces, preferred_element_type=jnp.float32
    )
    return jnp.sum(per_source.astype(jnp.bfloat16).astype(jnp.float32), axis=0)


def body(states, mix_weight, coherence, block_row, block_col, block_count, gain, bias):
    blocks = coherence[0, 0]
    row_ids = block_row[0, 0]
    col_ids = block_col[0, 0]
    live_count = block_count[0, 0]
    row_groups = lax.axis_size(("rx", "rc"))
    slot_total = row_ids.shape[0]
    seats_per_row = max(2, (slot_total + row_groups - 1) // row_groups)
    seat_blocks, seat_cols = seat_layout(
        blocks, row_ids, col_ids, live_count, row_groups, seats_per_row
    )
    owned_blocks = lax.all_to_all(seat_blocks, ("rx", "rc"), split_axis=0, concat_axis=0, tiled=True)
    owned_cols = lax.all_to_all(seat_cols, ("rx", "rc"), split_axis=0, concat_axis=0, tiled=True)
    hidden = to_grid(states)
    for iteration in range(ITERS):
        mixed = jnp.dot(hidden, mix_weight, preferred_element_type=jnp.float32).astype(jnp.bfloat16)
        coupled = couple(mixed, owned_blocks, owned_cols)
        hidden = normalize(hidden, coupled, gain, bias)
    return to_grid(hidden)


def solution(mesh):
    chips = mesh.devices.shape[0] // 2
    col_hi = 8 if mesh.devices.shape[1] % 8 == 0 else 1
    fine = jax.sharding.Mesh(
        mesh.devices.reshape(chips, 2, col_hi, mesh.devices.shape[1] // col_hi),
        ("rx", "rc", "cz", "cy"),
    )
    rows = ("rx", "rc")
    cols = ("cz", "cy")
    placed = (
        P(rows + cols, None),
        P(),
        P(rows, cols, None, None, None),
        P(rows, cols, None),
        P(rows, cols, None),
        P(rows, cols),
        P(),
        P(),
    )
    return jax.shard_map(
        body, mesh=fine, in_specs=placed, out_specs=P(rows + cols, None), check_vma=False
    )
```

```python
import jax
import jax.numpy as jnp
from jax import lax
from jax.sharding import PartitionSpec as P

ITERS = 2


def normalize(hidden, coupled, gain, bias):
    summed_in = hidden.astype(jnp.float32) + coupled
    mean_value = jnp.mean(summed_in, axis=-1, keepdims=True)
    centered = summed_in - mean_value
    variance = jnp.mean(centered * centered, axis=-1, keepdims=True)
    return (centered * lax.rsqrt(variance + 1e-05) * gain + bias).astype(jnp.bfloat16)


def to_grid(values):
    return lax.all_to_all(values, "col", split_axis=0, concat_axis=0, tiled=True)


def seat_layout(blocks, row_ids, col_ids, live_count, row_groups, seats_per_row):
    slot_total = row_ids.shape[0]
    block_len = blocks.shape[1]
    slot_ids = jnp.arange(slot_total, dtype=jnp.int32)
    live_mask = slot_ids < live_count
    earlier = (
        (row_ids[:, None] == row_ids[None, :])
        & (slot_ids[None, :] < slot_ids[:, None])
        & live_mask[None, :]
    )
    rank_in_row = jnp.sum(earlier.astype(jnp.int32), axis=1)
    seat_total = row_groups * seats_per_row
    seat_index = jnp.where(live_mask, row_ids * seats_per_row + rank_in_row, seat_total)
    seat_blocks = (
        jnp.zeros((seat_total, block_len, block_len), blocks.dtype)
        .at[seat_index]
        .set(blocks, mode="drop")
    )
    seat_cols = jnp.zeros((seat_total,), jnp.int32).at[seat_index].set(col_ids, mode="drop")
    return (
        seat_blocks.reshape(row_groups, seats_per_row, block_len, block_len),
        seat_cols.reshape(row_groups, seats_per_row),
    )


def couple(grid_mixed, owned_blocks, owned_cols):
    pieces_all = lax.all_gather(grid_mixed, "row", axis=0, tiled=False)
    pieces = pieces_all[owned_cols]
    per_source = jnp.einsum(
        "rsab,rsbh->rah", owned_blocks, pieces, preferred_element_type=jnp.float32
    )
    return jnp.sum(per_source.astype(jnp.bfloat16).astype(jnp.float32), axis=0)


def mix_and_couple(hidden, mix_weight, owned_blocks, owned_cols, chunks):
    width = mix_weight.shape[1] // chunks
    parts = []
    for chunk in range(chunks):
        weight = mix_weight[:, chunk * width:(chunk + 1) * width]
        mixed = jnp.dot(hidden, weight, preferred_element_type=jnp.float32).astype(jnp.bfloat16)
        parts.append(couple(mixed, owned_blocks, owned_cols))
    return jnp.concatenate(parts, axis=-1)


def body(states, mix_weight, coherence, block_row, block_col, block_count, gain, bias):
    blocks = coherence[0, 0]
    row_ids = block_row[0, 0]
    col_ids = block_col[0, 0]
    live_count = block_count[0, 0]
    row_groups = lax.axis_size("row")
    slot_total = row_ids.shape[0]
    seats_per_row = max(2, (slot_total + row_groups - 1) // row_groups)
    seat_blocks, seat_cols = seat_layout(
        blocks, row_ids, col_ids, live_count, row_groups, seats_per_row
    )
    states, seat_blocks, seat_cols = lax.optimization_barrier((states, seat_blocks, seat_cols))
    owned_blocks = lax.all_to_all(seat_blocks, "row", split_axis=0, concat_axis=0, tiled=True)
    owned_cols = lax.all_to_all(seat_cols, "row", split_axis=0, concat_axis=0, tiled=True)
    hidden = to_grid(states)
    for iteration in range(ITERS):
        coupled = mix_and_couple(hidden, mix_weight, owned_blocks, owned_cols, 2)
        hidden = normalize(hidden, coupled, gain, bias)
    return to_grid(hidden)


def solution(mesh):
    placed = (
        P(("row", "col"), None),
        P(),
        P("row", "col", None, None, None),
        P("row", "col", None),
        P("row", "col", None),
        P("row", "col"),
        P(),
        P(),
    )
    return jax.shard_map(
        body, mesh=mesh, in_specs=placed, out_specs=P(("row", "col"), None), check_vma=False
    )
```

```python
import jax
import jax.numpy as jnp
from jax import lax
from jax.sharding import PartitionSpec as P


ITERS = 2


def normalize(hidden, coupled, gain, bias):
    summed_in = hidden.astype(jnp.float32) + coupled
    mean_value = jnp.mean(summed_in, axis=-1, keepdims=True)
    centered = summed_in - mean_value
    variance = jnp.mean(centered * centered, axis=-1, keepdims=True)
    return (centered * lax.rsqrt(variance + 1e-05) * gain + bias).astype(jnp.bfloat16)


def to_grid(values):
    return lax.all_to_all(values, "col", split_axis=0, concat_axis=0, tiled=True)


def send_rows(bundle, row_groups):
    me = lax.axis_index("row")
    received = [lax.dynamic_index_in_dim(bundle, me, 0, keepdims=False)]
    for shift in range(1, row_groups):
        outgoing = lax.dynamic_index_in_dim(bundle, (me + shift) % row_groups, 0, keepdims=False)
        pairs = [(source, (source + shift) % row_groups) for source in range(row_groups)]
        received.append(lax.ppermute(outgoing, "row", pairs))
    return jnp.stack(received)


def seat_layout(blocks, row_ids, col_ids, live_count, row_groups, seats_per_row):
    slot_total = row_ids.shape[0]
    block_len = blocks.shape[1]
    slot_ids = jnp.arange(slot_total, dtype=jnp.int32)
    live_mask = slot_ids < live_count
    earlier = (
        (row_ids[:, None] == row_ids[None, :])
        & (slot_ids[None, :] < slot_ids[:, None])
        & live_mask[None, :]
    )
    rank_in_row = jnp.sum(earlier.astype(jnp.int32), axis=1)
    seat_total = row_groups * seats_per_row
    seat_index = jnp.where(live_mask, row_ids * seats_per_row + rank_in_row, seat_total)
    seat_blocks = (
        jnp.zeros((seat_total, block_len, block_len), blocks.dtype)
        .at[seat_index]
        .set(blocks, mode="drop")
    )
    seat_cols = jnp.zeros((seat_total,), jnp.int32).at[seat_index].set(col_ids, mode="drop")
    return (
        seat_blocks.reshape(row_groups, seats_per_row, block_len, block_len),
        seat_cols.reshape(row_groups, seats_per_row),
    )


def couple(grid_mixed, owned_blocks, owned_cols):
    pieces_all = lax.all_gather(grid_mixed, "row", axis=0, tiled=False)
    pieces = pieces_all[owned_cols]
    per_source = jnp.einsum(
        "rsab,rsbh->rah", owned_blocks, pieces, preferred_element_type=jnp.float32
    )
    return jnp.sum(per_source.astype(jnp.bfloat16).astype(jnp.float32), axis=0)


def mix_and_couple(hidden, mix_weight, owned_blocks, owned_cols, chunks):
    width = mix_weight.shape[1] // chunks
    parts = []
    for chunk in range(chunks):
        weight = mix_weight[:, chunk * width:(chunk + 1) * width]
        mixed = jnp.dot(hidden, weight, preferred_element_type=jnp.float32).astype(jnp.bfloat16)
        parts.append(couple(mixed, owned_blocks, owned_cols))
    return jnp.concatenate(parts, axis=-1)


def layer(states, mix_weight, coherence, block_row, block_col, block_count, gain, bias):
    blocks = coherence[0, 0]
    row_ids = block_row[0, 0]
    col_ids = block_col[0, 0]
    live_count = block_count[0, 0]
    row_groups = lax.axis_size("row")
    slot_total = row_ids.shape[0]
    seats_per_row = max(2, (slot_total + row_groups - 1) // row_groups)
    seat_blocks, seat_cols = seat_layout(
        blocks, row_ids, col_ids, live_count, row_groups, seats_per_row
    )
    states, seat_blocks, seat_cols = lax.optimization_barrier((states, seat_blocks, seat_cols))
    block_len = blocks.shape[-1]
    tail = 16
    col_rows = jnp.broadcast_to(
        seat_cols.astype(blocks.dtype)[:, :, None], (row_groups, seats_per_row, block_len)
    )
    col_rows = jnp.pad(col_rows, ((0, 0), (0, tail - seats_per_row), (0, 0)))
    bundle = jnp.concatenate(
        [seat_blocks.reshape(row_groups, seats_per_row * block_len, block_len), col_rows], axis=1
    )
    bundle = send_rows(bundle, row_groups)
    owned_blocks = bundle[:, : seats_per_row * block_len].reshape(seat_blocks.shape)
    owned_cols = bundle[:, seats_per_row * block_len : seats_per_row * block_len + seats_per_row, 0]
    owned_cols = owned_cols.astype(jnp.int32)
    hidden = to_grid(states)
    for _ in range(ITERS):
        coupled = mix_and_couple(hidden, mix_weight, owned_blocks, owned_cols, 2)
        hidden = normalize(hidden, coupled, gain, bias)
    return to_grid(hidden)


def solution(mesh):
    placed = (
        P(("row", "col"), None),
        P(),
        P("row", "col", None, None, None),
        P("row", "col", None),
        P("row", "col", None),
        P("row", "col"),
        P(),
        P(),
    )
    return jax.shard_map(
        layer, mesh=mesh, in_specs=placed, out_specs=P(("row", "col"), None), check_vma=False
    )
```

```python
import jax
import jax.numpy as jnp
from jax import lax
from jax.sharding import PartitionSpec as P

ITERS = 2


def normalize(hidden, coupled, gain, bias):
    summed_in = hidden.astype(jnp.float32) + coupled
    mean_value = jnp.mean(summed_in, axis=-1, keepdims=True)
    centered = summed_in - mean_value
    variance = jnp.mean(centered * centered, axis=-1, keepdims=True)
    return (centered * lax.rsqrt(variance + 1e-05) * gain + bias).astype(jnp.bfloat16)


def to_grid(values):
    return lax.all_to_all(values, "col", split_axis=0, concat_axis=0, tiled=True)


def seat_layout(blocks, row_ids, col_ids, live_count, row_groups, seats_per_row):
    slot_total = row_ids.shape[0]
    block_len = blocks.shape[1]
    slot_ids = jnp.arange(slot_total, dtype=jnp.int32)
    live_mask = slot_ids < live_count
    earlier = (
        (row_ids[:, None] == row_ids[None, :])
        & (slot_ids[None, :] < slot_ids[:, None])
        & live_mask[None, :]
    )
    rank_in_row = jnp.sum(earlier.astype(jnp.int32), axis=1)
    seat_total = row_groups * seats_per_row
    seat_index = jnp.where(live_mask, row_ids * seats_per_row + rank_in_row, seat_total)
    seat_blocks = (
        jnp.zeros((seat_total, block_len, block_len), blocks.dtype)
        .at[seat_index]
        .set(blocks, mode="drop")
    )
    seat_cols = jnp.zeros((seat_total,), jnp.int32).at[seat_index].set(col_ids, mode="drop")
    return (
        seat_blocks.reshape(row_groups, seats_per_row, block_len, block_len),
        seat_cols.reshape(row_groups, seats_per_row),
    )


def couple(grid_mixed, owned_blocks, owned_cols):
    pieces_all = lax.all_gather(grid_mixed, "row", axis=0, tiled=False)
    pieces = pieces_all[owned_cols]
    per_source = jnp.einsum(
        "rsab,rsbh->rah", owned_blocks, pieces, preferred_element_type=jnp.float32
    )
    return jnp.sum(per_source.astype(jnp.bfloat16).astype(jnp.float32), axis=0)


def body(states, mix_weight, coherence, block_row, block_col, block_count, gain, bias):
    blocks = coherence[0, 0]
    row_ids = block_row[0, 0]
    col_ids = block_col[0, 0]
    live_count = block_count[0, 0]
    row_groups = lax.axis_size("row")
    slot_total = row_ids.shape[0]
    seats_per_row = max(2, (slot_total + row_groups - 1) // row_groups)
    seat_blocks, seat_cols = seat_layout(
        blocks, row_ids, col_ids, live_count, row_groups, seats_per_row
    )
    block_len = blocks.shape[-1]
    tail = 16
    col_rows = jnp.broadcast_to(
        seat_cols.astype(blocks.dtype)[:, :, None], (row_groups, seats_per_row, block_len)
    )
    col_rows = jnp.pad(col_rows, ((0, 0), (0, tail - seats_per_row), (0, 0)))
    bundle = jnp.concatenate(
        [seat_blocks.reshape(row_groups, seats_per_row * block_len, block_len), col_rows], axis=1
    )
    bundle = lax.all_to_all(bundle, "row", split_axis=0, concat_axis=0, tiled=True)
    owned_blocks = bundle[:, : seats_per_row * block_len].reshape(seat_blocks.shape)
    owned_cols = bundle[:, seats_per_row * block_len : seats_per_row * block_len + seats_per_row, 0]
    owned_cols = owned_cols.astype(jnp.int32)
    hidden = to_grid(states)
    for iteration in range(ITERS):
        mixed = jnp.dot(hidden, mix_weight, preferred_element_type=jnp.float32).astype(jnp.bfloat16)
        coupled = couple(mixed, owned_blocks, owned_cols)
        hidden = normalize(hidden, coupled, gain, bias)
    return to_grid(hidden)


def solution(mesh):
    placed = (
        P(("row", "col"), None),
        P(),
        P("row", "col", None, None, None),
        P("row", "col", None),
        P("row", "col", None),
        P("row", "col"),
        P(),
        P(),
    )
    return jax.shard_map(
        body, mesh=mesh, in_specs=placed, out_specs=P(("row", "col"), None), check_vma=False
    )
```

```python
import jax
import jax.numpy as jnp
from jax import lax
from jax.experimental import pallas as pl
from jax.experimental.pallas import tpu as pltpu
from jax.sharding import PartitionSpec as P

ITERS = 2


def normalize(hidden, coupled, gain, bias):
    summed_in = hidden.astype(jnp.float32) + coupled
    mean_value = jnp.mean(summed_in, axis=-1, keepdims=True)
    centered = summed_in - mean_value
    variance = jnp.mean(centered * centered, axis=-1, keepdims=True)
    return (centered * lax.rsqrt(variance + 1e-05) * gain + bias).astype(jnp.bfloat16)


def to_grid(values):
    return lax.all_to_all(values, "col", split_axis=0, concat_axis=0, tiled=True)


def seat_layout(blocks, row_ids, col_ids, live_count, row_groups, seats_per_row):
    slot_total = row_ids.shape[0]
    block_len = blocks.shape[1]
    slot_ids = jnp.arange(slot_total, dtype=jnp.int32)
    live_mask = slot_ids < live_count
    earlier = (
        (row_ids[:, None] == row_ids[None, :])
        & (slot_ids[None, :] < slot_ids[:, None])
        & live_mask[None, :]
    )
    rank_in_row = jnp.sum(earlier.astype(jnp.int32), axis=1)
    seat_total = row_groups * seats_per_row
    seat_index = jnp.where(live_mask, row_ids * seats_per_row + rank_in_row, seat_total)
    seat_blocks = (
        jnp.zeros((seat_total, block_len, block_len), blocks.dtype)
        .at[seat_index]
        .set(blocks, mode="drop")
    )
    seat_cols = jnp.zeros((seat_total,), jnp.int32).at[seat_index].set(col_ids, mode="drop")
    return (
        seat_blocks.reshape(row_groups, seats_per_row, block_len, block_len),
        seat_cols.reshape(row_groups, seats_per_row),
    )


def couple(grid_mixed, owned_blocks, owned_cols):
    pieces_all = lax.all_gather(grid_mixed, "row", axis=0, tiled=False)
    pieces = pieces_all[owned_cols]
    per_source = jnp.einsum(
        "rsab,rsbh->rah", owned_blocks, pieces, preferred_element_type=jnp.float32
    )
    return jnp.sum(per_source.astype(jnp.bfloat16).astype(jnp.float32), axis=0)


def couple_kernel(cols_ref, blocks_ref, pieces_ref, hidden_ref, weight_ref, gain_ref, bias_ref,
                  hidden_out, mixed_out):
    sources, seats = blocks_ref.shape[0], blocks_ref.shape[1]

    def source_term(source, total):
        term = None
        for seat in range(seats):
            piece = pieces_ref[cols_ref[source * seats + seat]]
            product = jnp.dot(blocks_ref[source, seat], piece, preferred_element_type=jnp.float32)
            term = product if term is None else term + product
        return total + term.astype(jnp.bfloat16).astype(jnp.float32)

    coupled = lax.fori_loop(0, sources, source_term, jnp.zeros(hidden_ref.shape, jnp.float32))
    hidden = normalize(hidden_ref[...], coupled, gain_ref[...], bias_ref[...])
    hidden_out[...] = hidden
    mixed_out[...] = jnp.dot(
        hidden, weight_ref[...], preferred_element_type=jnp.float32
    ).astype(jnp.bfloat16)


def couple_step(pieces_all, owned_blocks, owned_cols, hidden, mix_weight, gain, bias):
    vmem = pl.BlockSpec(memory_space=pltpu.VMEM)
    return pl.pallas_call(
        couple_kernel,
        out_shape=(
            jax.ShapeDtypeStruct(hidden.shape, jnp.bfloat16),
            jax.ShapeDtypeStruct(hidden.shape, jnp.bfloat16),
        ),
        in_specs=[pl.BlockSpec(memory_space=pltpu.SMEM)] + [vmem] * 6,
        out_specs=(vmem, vmem),
    )(
        owned_cols.reshape(-1),
        owned_blocks,
        pieces_all,
        hidden,
        mix_weight,
        gain.reshape(1, -1),
        bias.reshape(1, -1),
    )


def body(states, mix_weight, coherence, block_row, block_col, block_count, gain, bias):
    blocks = coherence[0, 0]
    row_ids = block_row[0, 0]
    col_ids = block_col[0, 0]
    live_count = block_count[0, 0]
    row_groups = lax.axis_size("row")
    slot_total = row_ids.shape[0]
    seats_per_row = max(2, (slot_total + row_groups - 1) // row_groups)
    seat_blocks, seat_cols = seat_layout(
        blocks, row_ids, col_ids, live_count, row_groups, seats_per_row
    )
    block_len = blocks.shape[-1]
    tail = 16
    col_rows = jnp.broadcast_to(
        seat_cols.astype(blocks.dtype)[:, :, None], (row_groups, seats_per_row, block_len)
    )
    col_rows = jnp.pad(col_rows, ((0, 0), (0, tail - seats_per_row), (0, 0)))
    bundle = jnp.concatenate(
        [seat_blocks.reshape(row_groups, seats_per_row * block_len, block_len), col_rows], axis=1
    )
    bundle = lax.all_to_all(bundle, "row", split_axis=0, concat_axis=0, tiled=True)
    owned_blocks = bundle[:, : seats_per_row * block_len].reshape(seat_blocks.shape)
    owned_cols = bundle[:, seats_per_row * block_len : seats_per_row * block_len + seats_per_row, 0]
    owned_cols = owned_cols.astype(jnp.int32)
    hidden = to_grid(states)
    mixed = jnp.dot(hidden, mix_weight, preferred_element_type=jnp.float32).astype(jnp.bfloat16)
    for iteration in range(ITERS):
        pieces_all = lax.all_gather(mixed, "row", axis=0, tiled=False)
        hidden, mixed = couple_step(
            pieces_all, owned_blocks, owned_cols, hidden, mix_weight, gain, bias
        )
    return to_grid(hidden)


def solution(mesh):
    placed = (
        P(("row", "col"), None),
        P(),
        P("row", "col", None, None, None),
        P("row", "col", None),
        P("row", "col", None),
        P("row", "col"),
        P(),
        P(),
    )
    return jax.shard_map(
        body, mesh=mesh, in_specs=placed, out_specs=P(("row", "col"), None), check_vma=False
    )
```

```python
import jax
import jax.numpy as jnp
from jax import lax
from jax.experimental import pallas as pl
from jax.experimental.pallas import tpu as pltpu
from jax.sharding import PartitionSpec as P

ITERS = 2


def normalize(hidden, coupled, gain, bias):
    summed_in = hidden.astype(jnp.float32) + coupled
    mean_value = jnp.mean(summed_in, axis=-1, keepdims=True)
    centered = summed_in - mean_value
    variance = jnp.mean(centered * centered, axis=-1, keepdims=True)
    return (centered * lax.rsqrt(variance + 1e-05) * gain + bias).astype(jnp.bfloat16)


def to_grid(values):
    return lax.all_to_all(values, "col", split_axis=0, concat_axis=0, tiled=True)


def seat_layout(blocks, row_ids, col_ids, live_count, row_groups, seats_per_row):
    slot_total = row_ids.shape[0]
    block_len = blocks.shape[1]
    slot_ids = jnp.arange(slot_total, dtype=jnp.int32)
    live_mask = slot_ids < live_count
    earlier = (
        (row_ids[:, None] == row_ids[None, :])
        & (slot_ids[None, :] < slot_ids[:, None])
        & live_mask[None, :]
    )
    rank_in_row = jnp.sum(earlier.astype(jnp.int32), axis=1)
    seat_total = row_groups * seats_per_row
    seat_index = jnp.where(live_mask, row_ids * seats_per_row + rank_in_row, seat_total)
    seat_blocks = (
        jnp.zeros((seat_total, block_len, block_len), blocks.dtype)
        .at[seat_index]
        .set(blocks, mode="drop")
    )
    seat_cols = jnp.zeros((seat_total,), jnp.int32).at[seat_index].set(col_ids, mode="drop")
    return (
        seat_blocks.reshape(row_groups, seats_per_row, block_len, block_len),
        seat_cols.reshape(row_groups, seats_per_row),
    )


def couple(grid_mixed, owned_blocks, owned_cols):
    pieces_all = lax.all_gather(grid_mixed, "row", axis=0, tiled=False)
    pieces = pieces_all[owned_cols]
    per_source = jnp.einsum(
        "rsab,rsbh->rah", owned_blocks, pieces, preferred_element_type=jnp.float32
    )
    return jnp.sum(per_source.astype(jnp.bfloat16).astype(jnp.float32), axis=0)


def couple_kernel(cols_ref, blocks_ref, pieces_ref, hidden_ref, weight_ref, gain_ref, bias_ref,
                  hidden_out, mixed_out):
    sources, seats = blocks_ref.shape[0], blocks_ref.shape[1]

    def source_term(source, total):
        term = None
        for seat in range(seats):
            piece = pieces_ref[cols_ref[source * seats + seat]]
            product = jnp.dot(blocks_ref[source, seat], piece, preferred_element_type=jnp.float32)
            term = product if term is None else term + product
        return total + term.astype(jnp.bfloat16).astype(jnp.float32)

    coupled = lax.fori_loop(0, sources, source_term, jnp.zeros(hidden_ref.shape, jnp.float32))
    hidden = normalize(hidden_ref[...], coupled, gain_ref[...], bias_ref[...])
    hidden_out[...] = hidden
    mixed_out[...] = jnp.dot(
        hidden, weight_ref[...], preferred_element_type=jnp.float32
    ).astype(jnp.bfloat16)


def couple_step(pieces_all, owned_blocks, owned_cols, hidden, mix_weight, gain, bias):
    vmem = pl.BlockSpec(memory_space=pltpu.VMEM)
    return pl.pallas_call(
        couple_kernel,
        out_shape=(
            jax.ShapeDtypeStruct(hidden.shape, jnp.bfloat16),
            jax.ShapeDtypeStruct(hidden.shape, jnp.bfloat16),
        ),
        in_specs=[pl.BlockSpec(memory_space=pltpu.SMEM)] + [vmem] * 6,
        out_specs=(vmem, vmem),
    )(
        owned_cols.reshape(-1),
        owned_blocks,
        pieces_all,
        hidden,
        mix_weight,
        gain.reshape(1, -1),
        bias.reshape(1, -1),
    )


def body(states, mix_weight, coherence, block_row, block_col, block_count, gain, bias):
    blocks = coherence[0, 0]
    row_ids = block_row[0, 0]
    col_ids = block_col[0, 0]
    live_count = block_count[0, 0]
    row_groups = lax.axis_size("row")
    slot_total = row_ids.shape[0]
    seats_per_row = max(2, (slot_total + row_groups - 1) // row_groups)
    seat_blocks, seat_cols = seat_layout(
        blocks, row_ids, col_ids, live_count, row_groups, seats_per_row
    )
    block_len = blocks.shape[-1]
    tail = 16
    col_rows = jnp.broadcast_to(
        seat_cols.astype(blocks.dtype)[:, :, None], (row_groups, seats_per_row, block_len)
    )
    col_rows = jnp.pad(col_rows, ((0, 0), (0, tail - seats_per_row), (0, 0)))
    bundle = jnp.concatenate(
        [seat_blocks.reshape(row_groups, seats_per_row * block_len, block_len), col_rows], axis=1
    )
    bundle = lax.all_to_all(bundle, "row", split_axis=0, concat_axis=0, tiled=True)
    owned_blocks = bundle[:, : seats_per_row * block_len].reshape(seat_blocks.shape)
    owned_cols = bundle[:, seats_per_row * block_len : seats_per_row * block_len + seats_per_row, 0]
    owned_cols = owned_cols.astype(jnp.int32)
    hidden = to_grid(states)
    mixed = jnp.dot(hidden, mix_weight, preferred_element_type=jnp.float32).astype(jnp.bfloat16)
    for iteration in range(ITERS):
        if iteration == 0:
            pieces_all = lax.all_gather(mixed, "row", axis=0, tiled=False)
        else:
            half = mixed.shape[-1] // 2
            pieces_all = jnp.concatenate(
                [
                    lax.all_gather(mixed[:, :half], "row", axis=0, tiled=False),
                    lax.all_gather(mixed[:, half:], "row", axis=0, tiled=False),
                ],
                axis=-1,
            )
        hidden, mixed = couple_step(
            pieces_all, owned_blocks, owned_cols, hidden, mix_weight, gain, bias
        )
    return to_grid(hidden)


def solution(mesh):
    placed = (
        P(("row", "col"), None),
        P(),
        P("row", "col", None, None, None),
        P("row", "col", None),
        P("row", "col", None),
        P("row", "col"),
        P(),
        P(),
    )
    return jax.shard_map(
        body, mesh=mesh, in_specs=placed, out_specs=P(("row", "col"), None), check_vma=False
    )
```

```python
import jax
import jax.numpy as jnp
from jax import lax
from jax.experimental import pallas as pl
from jax.experimental.pallas import tpu as pltpu
from jax.sharding import PartitionSpec as P

ITERS = 2


def normalize(hidden, coupled, gain, bias):
    summed_in = hidden.astype(jnp.float32) + coupled
    mean_value = jnp.mean(summed_in, axis=-1, keepdims=True)
    centered = summed_in - mean_value
    variance = jnp.mean(centered * centered, axis=-1, keepdims=True)
    return (centered * lax.rsqrt(variance + 1e-05) * gain + bias).astype(jnp.bfloat16)


def to_grid(values):
    return lax.all_to_all(values, "col", split_axis=0, concat_axis=0, tiled=True)


def seat_layout(blocks, row_ids, col_ids, live_count, row_groups, seats_per_row):
    slot_total = row_ids.shape[0]
    block_len = blocks.shape[1]
    slot_ids = jnp.arange(slot_total, dtype=jnp.int32)
    live_mask = slot_ids < live_count
    earlier = (
        (row_ids[:, None] == row_ids[None, :])
        & (slot_ids[None, :] < slot_ids[:, None])
        & live_mask[None, :]
    )
    rank_in_row = jnp.sum(earlier.astype(jnp.int32), axis=1)
    seat_total = row_groups * seats_per_row
    seat_index = jnp.where(live_mask, row_ids * seats_per_row + rank_in_row, seat_total)
    seat_blocks = (
        jnp.zeros((seat_total, block_len, block_len), blocks.dtype)
        .at[seat_index]
        .set(blocks, mode="drop")
    )
    seat_cols = jnp.zeros((seat_total,), jnp.int32).at[seat_index].set(col_ids, mode="drop")
    return (
        seat_blocks.reshape(row_groups, seats_per_row, block_len, block_len),
        seat_cols.reshape(row_groups, seats_per_row),
    )


def couple(grid_mixed, owned_blocks, owned_cols):
    pieces_all = lax.all_gather(grid_mixed, "row", axis=0, tiled=False)
    pieces = pieces_all[owned_cols]
    per_source = jnp.einsum(
        "rsab,rsbh->rah", owned_blocks, pieces, preferred_element_type=jnp.float32
    )
    return jnp.sum(per_source.astype(jnp.bfloat16).astype(jnp.float32), axis=0)


def couple_kernel(cols_ref, bundle_ref, pieces_ref, hidden_ref, weight_ref, gain_ref, bias_ref,
                  hidden_out, *mixed_out):
    sources = bundle_ref.shape[0]
    block_len = hidden_ref.shape[0]
    seats = cols_ref.shape[0] // sources

    def source_term(source, total):
        term = None
        for seat in range(seats):
            piece = pieces_ref[cols_ref[source * seats + seat]]
            block = bundle_ref[source, seat * block_len:(seat + 1) * block_len, :]
            product = jnp.dot(block, piece, preferred_element_type=jnp.float32)
            term = product if term is None else term + product
        return total + term.astype(jnp.bfloat16).astype(jnp.float32)

    coupled = lax.fori_loop(0, sources, source_term, jnp.zeros(hidden_ref.shape, jnp.float32))
    hidden = normalize(hidden_ref[...], coupled, gain_ref[...], bias_ref[...])
    hidden_out[...] = hidden
    for out in mixed_out:
        out[...] = jnp.dot(hidden, weight_ref[...], preferred_element_type=jnp.float32).astype(
            jnp.bfloat16
        )


def couple_step(pieces_all, bundle, owned_cols, hidden, mix_weight, gain, bias, mix_next):
    vmem = pl.BlockSpec(memory_space=pltpu.VMEM)
    outs = 2 if mix_next else 1
    results = pl.pallas_call(
        couple_kernel,
        out_shape=tuple(jax.ShapeDtypeStruct(hidden.shape, jnp.bfloat16) for _ in range(outs)),
        in_specs=[pl.BlockSpec(memory_space=pltpu.SMEM)] + [vmem] * 6,
        out_specs=tuple(vmem for _ in range(outs)),
    )(
        owned_cols.reshape(-1),
        bundle,
        pieces_all,
        hidden,
        mix_weight,
        gain.reshape(1, -1),
        bias.reshape(1, -1),
    )
    return results if mix_next else (results[0], None)


def body(states, mix_weight, coherence, block_row, block_col, block_count, gain, bias):
    blocks = coherence[0, 0]
    row_ids = block_row[0, 0]
    col_ids = block_col[0, 0]
    live_count = block_count[0, 0]
    row_groups = lax.axis_size("row")
    slot_total = row_ids.shape[0]
    seats_per_row = max(2, (slot_total + row_groups - 1) // row_groups)
    seat_blocks, seat_cols = seat_layout(
        blocks, row_ids, col_ids, live_count, row_groups, seats_per_row
    )
    block_len = blocks.shape[-1]
    tail = 16
    col_rows = jnp.broadcast_to(
        seat_cols.astype(blocks.dtype)[:, :, None], (row_groups, seats_per_row, block_len)
    )
    col_rows = jnp.pad(col_rows, ((0, 0), (0, tail - seats_per_row), (0, 0)))
    bundle = jnp.concatenate(
        [seat_blocks.reshape(row_groups, seats_per_row * block_len, block_len), col_rows], axis=1
    )
    bundle = lax.all_to_all(bundle, "row", split_axis=0, concat_axis=0, tiled=True)
    owned_cols = bundle[:, seats_per_row * block_len : seats_per_row * block_len + seats_per_row, 0]
    owned_cols = owned_cols.astype(jnp.int32)
    hidden = to_grid(states)
    mixed = jnp.dot(hidden, mix_weight, preferred_element_type=jnp.float32).astype(jnp.bfloat16)
    for iteration in range(ITERS):
        if iteration == 0:
            pieces_all = lax.all_gather(mixed, "row", axis=0, tiled=False)
        else:
            half = mixed.shape[-1] // 2
            pieces_all = jnp.concatenate(
                [
                    lax.all_gather(mixed[:, :half], "row", axis=0, tiled=False),
                    lax.all_gather(mixed[:, half:], "row", axis=0, tiled=False),
                ],
                axis=-1,
            )
        hidden, mixed = couple_step(
            pieces_all, bundle, owned_cols, hidden, mix_weight, gain, bias, iteration + 1 < ITERS
        )
    return to_grid(hidden)


def solution(mesh):
    placed = (
        P(("row", "col"), None),
        P(),
        P("row", "col", None, None, None),
        P("row", "col", None),
        P("row", "col", None),
        P("row", "col"),
        P(),
        P(),
    )
    return jax.shard_map(
        body, mesh=mesh, in_specs=placed, out_specs=P(("row", "col"), None), check_vma=False
    )
```

```python
import jax
import jax.numpy as jnp
from jax import lax
from jax.experimental import pallas as pl
from jax.experimental.pallas import tpu as pltpu
from jax.sharding import PartitionSpec as P

ITERS = 2


def normalize(hidden, coupled, gain, bias):
    summed_in = hidden.astype(jnp.float32) + coupled
    mean_value = jnp.mean(summed_in, axis=-1, keepdims=True)
    centered = summed_in - mean_value
    variance = jnp.mean(centered * centered, axis=-1, keepdims=True)
    return (centered * lax.rsqrt(variance + 1e-05) * gain + bias).astype(jnp.bfloat16)


def to_grid(values):
    return lax.all_to_all(values, "col", split_axis=0, concat_axis=0, tiled=True)


def seat_layout(blocks, row_ids, col_ids, live_count, row_groups, seats_per_row):
    slot_total = row_ids.shape[0]
    block_len = blocks.shape[1]
    slot_ids = jnp.arange(slot_total, dtype=jnp.int32)
    live_mask = slot_ids < live_count
    earlier = (
        (row_ids[:, None] == row_ids[None, :])
        & (slot_ids[None, :] < slot_ids[:, None])
        & live_mask[None, :]
    )
    rank_in_row = jnp.sum(earlier.astype(jnp.int32), axis=1)
    seat_total = row_groups * seats_per_row
    seat_index = jnp.where(live_mask, row_ids * seats_per_row + rank_in_row, seat_total)
    seat_blocks = (
        jnp.zeros((seat_total, block_len, block_len), blocks.dtype)
        .at[seat_index]
        .set(blocks, mode="drop")
    )
    seat_cols = jnp.zeros((seat_total,), jnp.int32).at[seat_index].set(col_ids, mode="drop")
    return (
        seat_blocks.reshape(row_groups, seats_per_row, block_len, block_len),
        seat_cols.reshape(row_groups, seats_per_row),
    )


def couple(grid_mixed, owned_blocks, owned_cols):
    pieces_all = lax.all_gather(grid_mixed, "row", axis=0, tiled=False)
    pieces = pieces_all[owned_cols]
    per_source = jnp.einsum(
        "rsab,rsbh->rah", owned_blocks, pieces, preferred_element_type=jnp.float32
    )
    return jnp.sum(per_source.astype(jnp.bfloat16).astype(jnp.float32), axis=0)


def couple_kernel(cols_ref, bundle_ref, pieces_ref, hidden_ref, weight_ref, gain_ref, bias_ref,
                  hidden_out, *mixed_out):
    sources = bundle_ref.shape[0]
    block_len = hidden_ref.shape[0]
    seats = cols_ref.shape[0] // sources

    def source_term(source, total):
        term = None
        for seat in range(seats):
            piece = pieces_ref[cols_ref[source * seats + seat]]
            block = bundle_ref[source, seat * block_len:(seat + 1) * block_len, :]
            product = jnp.dot(block, piece, preferred_element_type=jnp.float32)
            term = product if term is None else term + product
        return total + term.astype(jnp.bfloat16).astype(jnp.float32)

    coupled = lax.fori_loop(
        0, sources, source_term, jnp.zeros(hidden_ref.shape, jnp.float32), unroll=True
    )
    hidden = normalize(hidden_ref[...], coupled, gain_ref[...], bias_ref[...])
    hidden_out[...] = hidden
    for out in mixed_out:
        out[...] = jnp.dot(hidden, weight_ref[...], preferred_element_type=jnp.float32).astype(
            jnp.bfloat16
        )


def couple_step(pieces_all, bundle, owned_cols, hidden, mix_weight, gain, bias, mix_next):
    vmem = pl.BlockSpec(memory_space=pltpu.VMEM)
    outs = 2 if mix_next else 1
    results = pl.pallas_call(
        couple_kernel,
        out_shape=tuple(jax.ShapeDtypeStruct(hidden.shape, jnp.bfloat16) for _ in range(outs)),
        in_specs=[pl.BlockSpec(memory_space=pltpu.SMEM)] + [vmem] * 6,
        out_specs=tuple(vmem for _ in range(outs)),
    )(
        owned_cols.reshape(-1),
        bundle,
        pieces_all,
        hidden,
        mix_weight,
        gain.reshape(1, -1),
        bias.reshape(1, -1),
    )
    return results if mix_next else (results[0], None)


def body(states, mix_weight, coherence, block_row, block_col, block_count, gain, bias):
    blocks = coherence[0, 0]
    row_ids = block_row[0, 0]
    col_ids = block_col[0, 0]
    live_count = block_count[0, 0]
    row_groups = lax.axis_size("row")
    slot_total = row_ids.shape[0]
    seats_per_row = max(2, (slot_total + row_groups - 1) // row_groups)
    seat_blocks, seat_cols = seat_layout(
        blocks, row_ids, col_ids, live_count, row_groups, seats_per_row
    )
    block_len = blocks.shape[-1]
    tail = 16
    col_rows = jnp.broadcast_to(
        seat_cols.astype(blocks.dtype)[:, :, None], (row_groups, seats_per_row, block_len)
    )
    col_rows = jnp.pad(col_rows, ((0, 0), (0, tail - seats_per_row), (0, 0)))
    bundle = jnp.concatenate(
        [seat_blocks.reshape(row_groups, seats_per_row * block_len, block_len), col_rows], axis=1
    )
    bundle = lax.all_to_all(bundle, "row", split_axis=0, concat_axis=0, tiled=True)
    owned_cols = bundle[:, seats_per_row * block_len : seats_per_row * block_len + seats_per_row, 0]
    owned_cols = owned_cols.astype(jnp.int32)
    hidden = to_grid(states)
    mixed = jnp.dot(hidden, mix_weight, preferred_element_type=jnp.float32).astype(jnp.bfloat16)
    for iteration in range(ITERS):
        if iteration == 0:
            pieces_all = lax.all_gather(mixed, "row", axis=0, tiled=False)
        else:
            half = mixed.shape[-1] // 2
            pieces_all = jnp.concatenate(
                [
                    lax.all_gather(mixed[:, :half], "row", axis=0, tiled=False),
                    lax.all_gather(mixed[:, half:], "row", axis=0, tiled=False),
                ],
                axis=-1,
            )
        hidden, mixed = couple_step(
            pieces_all, bundle, owned_cols, hidden, mix_weight, gain, bias, iteration + 1 < ITERS
        )
    return to_grid(hidden)


def solution(mesh):
    placed = (
        P(("row", "col"), None),
        P(),
        P("row", "col", None, None, None),
        P("row", "col", None),
        P("row", "col", None),
        P("row", "col"),
        P(),
        P(),
    )
    return jax.shard_map(
        body, mesh=mesh, in_specs=placed, out_specs=P(("row", "col"), None), check_vma=False
    )
```

```python
import jax
import jax.numpy as jnp
from jax import lax
from jax.experimental import pallas as pl
from jax.experimental.pallas import tpu as pltpu
from jax.sharding import PartitionSpec as P

ITERS = 2


def normalize(hidden, coupled, gain, bias):
    summed_in = hidden.astype(jnp.float32) + coupled
    mean_value = jnp.mean(summed_in, axis=-1, keepdims=True)
    centered = summed_in - mean_value
    variance = jnp.mean(centered * centered, axis=-1, keepdims=True)
    return (centered * lax.rsqrt(variance + 1e-05) * gain + bias).astype(jnp.bfloat16)


def to_grid(values):
    return lax.all_to_all(values, "col", split_axis=0, concat_axis=0, tiled=True)


def seat_layout(blocks, row_ids, col_ids, live_count, row_groups, seats_per_row):
    slot_total = row_ids.shape[0]
    block_len = blocks.shape[1]
    slot_ids = jnp.arange(slot_total, dtype=jnp.int32)
    live_mask = slot_ids < live_count
    earlier = (
        (row_ids[:, None] == row_ids[None, :])
        & (slot_ids[None, :] < slot_ids[:, None])
        & live_mask[None, :]
    )
    rank_in_row = jnp.sum(earlier.astype(jnp.int32), axis=1)
    seat_total = row_groups * seats_per_row
    seat_index = jnp.where(live_mask, row_ids * seats_per_row + rank_in_row, seat_total)
    seat_blocks = (
        jnp.zeros((seat_total, block_len, block_len), blocks.dtype)
        .at[seat_index]
        .set(blocks, mode="drop")
    )
    seat_cols = jnp.zeros((seat_total,), jnp.int32).at[seat_index].set(col_ids, mode="drop")
    return (
        seat_blocks.reshape(row_groups, seats_per_row, block_len, block_len),
        seat_cols.reshape(row_groups, seats_per_row),
    )


def couple(grid_mixed, owned_blocks, owned_cols):
    pieces_all = lax.all_gather(grid_mixed, "row", axis=0, tiled=False)
    pieces = pieces_all[owned_cols]
    per_source = jnp.einsum(
        "rsab,rsbh->rah", owned_blocks, pieces, preferred_element_type=jnp.float32
    )
    return jnp.sum(per_source.astype(jnp.bfloat16).astype(jnp.float32), axis=0)


def couple_kernel(cols_ref, bundle_ref, pieces_ref, hidden_ref, weight_ref, gain_ref, bias_ref,
                  hidden_out, *mixed_out):
    sources = bundle_ref.shape[0]
    block_len = hidden_ref.shape[0]
    seats = cols_ref.shape[0] // sources

    def source_term(source, total):
        block = jnp.concatenate(
            [bundle_ref[source, seat * block_len:(seat + 1) * block_len, :] for seat in range(seats)],
            axis=1,
        )
        piece = jnp.concatenate(
            [pieces_ref[cols_ref[source * seats + seat]] for seat in range(seats)], axis=0
        )
        term = jnp.dot(block, piece, preferred_element_type=jnp.float32)
        return total + term.astype(jnp.bfloat16).astype(jnp.float32)

    coupled = lax.fori_loop(
        0, sources, source_term, jnp.zeros(hidden_ref.shape, jnp.float32), unroll=True
    )
    hidden = normalize(hidden_ref[...], coupled, gain_ref[...], bias_ref[...])
    hidden_out[...] = hidden
    for out in mixed_out:
        out[...] = jnp.dot(hidden, weight_ref[...], preferred_element_type=jnp.float32).astype(
            jnp.bfloat16
        )


def couple_step(pieces_all, bundle, owned_cols, hidden, mix_weight, gain, bias, mix_next):
    vmem = pl.BlockSpec(memory_space=pltpu.VMEM)
    outs = 2 if mix_next else 1
    results = pl.pallas_call(
        couple_kernel,
        out_shape=tuple(jax.ShapeDtypeStruct(hidden.shape, jnp.bfloat16) for _ in range(outs)),
        in_specs=[pl.BlockSpec(memory_space=pltpu.SMEM)] + [vmem] * 6,
        out_specs=tuple(vmem for _ in range(outs)),
    )(
        owned_cols.reshape(-1),
        bundle,
        pieces_all,
        hidden,
        mix_weight,
        gain.reshape(1, -1),
        bias.reshape(1, -1),
    )
    return results if mix_next else (results[0], None)


def body(states, mix_weight, coherence, block_row, block_col, block_count, gain, bias):
    blocks = coherence[0, 0]
    row_ids = block_row[0, 0]
    col_ids = block_col[0, 0]
    live_count = block_count[0, 0]
    row_groups = lax.axis_size("row")
    slot_total = row_ids.shape[0]
    seats_per_row = max(2, (slot_total + row_groups - 1) // row_groups)
    seat_blocks, seat_cols = seat_layout(
        blocks, row_ids, col_ids, live_count, row_groups, seats_per_row
    )
    block_len = blocks.shape[-1]
    tail = 16
    col_rows = jnp.broadcast_to(
        seat_cols.astype(blocks.dtype)[:, :, None], (row_groups, seats_per_row, block_len)
    )
    col_rows = jnp.pad(col_rows, ((0, 0), (0, tail - seats_per_row), (0, 0)))
    bundle = jnp.concatenate(
        [seat_blocks.reshape(row_groups, seats_per_row * block_len, block_len), col_rows], axis=1
    )
    bundle = lax.all_to_all(bundle, "row", split_axis=0, concat_axis=0, tiled=True)
    owned_cols = bundle[:, seats_per_row * block_len : seats_per_row * block_len + seats_per_row, 0]
    owned_cols = owned_cols.astype(jnp.int32)
    hidden = to_grid(states)
    mixed = jnp.dot(hidden, mix_weight, preferred_element_type=jnp.float32).astype(jnp.bfloat16)
    for iteration in range(ITERS):
        if iteration == 0:
            pieces_all = lax.all_gather(mixed, "row", axis=0, tiled=False)
        else:
            half = mixed.shape[-1] // 2
            pieces_all = jnp.concatenate(
                [
                    lax.all_gather(mixed[:, :half], "row", axis=0, tiled=False),
                    lax.all_gather(mixed[:, half:], "row", axis=0, tiled=False),
                ],
                axis=-1,
            )
        hidden, mixed = couple_step(
            pieces_all, bundle, owned_cols, hidden, mix_weight, gain, bias, iteration + 1 < ITERS
        )
    return to_grid(hidden)


def solution(mesh):
    placed = (
        P(("row", "col"), None),
        P(),
        P("row", "col", None, None, None),
        P("row", "col", None),
        P("row", "col", None),
        P("row", "col"),
        P(),
        P(),
    )
    return jax.shard_map(
        body, mesh=mesh, in_specs=placed, out_specs=P(("row", "col"), None), check_vma=False
    )
```
